32 devices in a mesh: dp: 32 (over z, y, x, core), mp: 1.
Axes of the slice: x: 2, y: 2, z: 4, core: 2. Of those that a mesh axis runs over, the one named last changes fastest.
Arguments:
- context: bfloat16 [16384, 6144], P('dp', 'mp'), may hold values from -6 to 6
- weight: float32 [6144, 6144], P(('mp', 'dp')), may hold values from -0.078125 to 0.078125
- moment_one: float32 [6144, 6144], P(('mp', 'dp')), may hold values from -4 to 4
- moment_two: float32 [6144, 6144], P(('mp', 'dp')), may hold values from 0.05 to 2
- grad_out: bfloat16 [16384, 6144], P(('dp', 'mp')), may hold values from -6 to 6
Outputs:
- output: bfloat16 [16384, 6144], P(('dp', 'mp'))
- d_context: bfloat16 [16384, 6144], P('dp', 'mp')
- new_weight: float32 [6144, 6144], P(('mp', 'dp'))
- new_moment_one: float32 [6144, 6144], P(('mp', 'dp'))
- new_moment_two: float32 [6144, 6144], P(('mp', 'dp'))
The draws below stay inside these ranges and needn't reach their ends.
All inputs are finite; a program needn't handle non-finite values.
Results may differ from the reference program's by a relative error of at most 0.017.
Values may be sent and summed in bfloat16 or wider, within the bound.
No kernel may reach another device: no remote copies, remote signals or barrier semaphores. Data moves between devices by JAX's collectives and lax.ppermute only.
A program may use at most 192 MiB of HBM per device.

```python
import math
import jax
import jax.numpy as jnp
from jax import lax

D = 6144
TOK_DEV = 512
TOKENS = 16384
N_DP = 32
N_MP = 1


def spiked(values, own_key, source, target, shards_of, factor):
    owner, partner = [(jnp.arange(values.shape[dim]) // (values.shape[dim] // shards_of)).reshape([-1 if axis == dim else 1 for axis in range(values.ndim)]) for dim in (source, target)]
    chosen = jax.random.permutation(own_key, shards_of)[partner]
    strong = (owner == chosen) | (owner == (partner + shards_of // 2) % shards_of)
    return jnp.where(strong, factor * values, values)


def block_levels(own_key, extent, pieces, smallest, high):
    level, own = 1.0, jax.random.fold_in(own_key, 6)
    for dim, blocks in pieces:
        heights = jnp.exp(jax.random.uniform(jax.random.fold_in(own, dim), (blocks,), jnp.float32, smallest / len(pieces), high / len(pieces)))
        level = level * jnp.repeat(heights, extent[dim] // blocks).reshape([-1 if axis == dim else 1 for axis in range(len(extent))])
    return level


def centred(stream_key, extent, width, reach, cuts=(), kind=jnp.bfloat16):
    level = block_levels(stream_key, extent, cuts, -0.22, 0.18) if cuts else 1.0
    array = jax.random.normal(stream_key, extent, jnp.float32) * width * level
    return jnp.minimum(jnp.maximum(array, -reach), reach).astype(kind)


def gaussian_with(own_key, extent, deviation, bound, split, heavy, kind=jnp.bfloat16):
    array = deviation * jax.random.normal(own_key, extent, jnp.float32)
    if split:
        array = array * block_levels(own_key, extent, split, -0.22, 0.18)
    return jnp.clip(spiked(array, jax.random.fold_in(own_key, 3), *heavy), -bound, bound).astype(kind)


def setup_inputs(seed: int = 0) -> dict:
    seeds = jax.random.split(jax.random.key(seed), 6)
    return {
        "context": gaussian_with(seeds[0], (TOKENS, D), 1.0, 6.0, ((0, 32),), (0, 1, 32, 2.75)),
        "weight": centred(seeds[1], (D, D), D ** -0.5, 0.078125, ((0, 32),), jnp.float32),
        "moment_one": centred(seeds[2], (D, D), 0.3, 4.0, ((0, 32),), jnp.float32),
        "moment_two": jnp.clip(jnp.exp(math.log(2.0) - 3.6888794 * jax.random.uniform(seeds[3], (D, D), jnp.float32) ** block_levels(seeds[3], (D, D), ((0, 32),), -0.2, 0.2)), 0.05, 2.0),
        "grad_out": gaussian_with(seeds[4], (TOKENS, D), 1.0, 6.0, ((0, 32),), (0, 1, 32, 2.75)),
    }


def reference(context, weight, moment_one, moment_two, grad_out):
    weight_bf = weight.astype(jnp.bfloat16)
    group = D // N_MP
    summed = jnp.zeros((TOKENS, D), jnp.float32)
    for k in range(N_MP):
        partial_k = jnp.dot(context[:, k * group:(k + 1) * group], weight_bf[k * group:(k + 1) * group, :], preferred_element_type=jnp.float32)
        summed = summed + lax.optimization_barrier(partial_k.astype(jnp.bfloat16)).astype(jnp.float32)
    output = summed.astype(jnp.bfloat16)
    d_context = lax.dot_general(grad_out, weight_bf, (((1,), (1,)), ((), ())), preferred_element_type=jnp.float32).astype(jnp.bfloat16)
    ctx_blocks = context.reshape(N_DP, TOK_DEV, D)
    cot_blocks = grad_out.reshape(N_DP, TOK_DEV, D)

    def add_block(total, pair):
        block_grad = lax.dot_general(pair[0], pair[1], (((0,), (0,)), ((), ())), preferred_element_type=jnp.float32)
        return (total + lax.optimization_barrier(block_grad.astype(jnp.bfloat16)).astype(jnp.float32), None)
    total, unused = lax.scan(add_block, jnp.zeros((D, D), jnp.float32), (ctx_blocks, cot_blocks))
    grad = total * (1.0 / math.sqrt(TOKENS))
    new_moment_one = 0.9 * moment_one + 0.1 * grad
    new_moment_two = 0.999 * moment_two + 0.001 * grad * grad
    first_fix = 1.0 - 0.9 ** 10
    second_fix = 1.0 - 0.999 ** 10
    update = new_moment_one / first_fix / (jnp.sqrt(new_moment_two / second_fix) + 1e-08) + 0.1 * weight
    new_weight = weight - 0.001 * update
    return (output, d_context, new_weight, new_moment_one, new_moment_two)
```

```python
import math

import jax
import jax.numpy as jnp
from jax import lax
from jax.sharding import PartitionSpec as P

GRAD_CHUNKS = 4


def per_device(context, weight, moment_one, moment_two, grad_out):
    weight_bf, weight = lax.optimization_barrier((weight.astype(jnp.bfloat16), weight))
    tok_rows = context.shape[0]
    full_weight = lax.all_gather(weight_bf, "dp", axis=0, tiled=True)
    partials = jnp.dot(context, full_weight, preferred_element_type=jnp.float32)
    summed = lax.psum_scatter(partials.astype(jnp.bfloat16), "mp", scatter_dimension=0, tiled=True)
    piece = lax.all_gather(grad_out, "mp", axis=0, tiled=True)
    back_rows = lax.dot_general(
        piece, full_weight, (((1,), (1,)), ((), ())), preferred_element_type=jnp.float32
    )
    d_context = back_rows.astype(jnp.bfloat16)
    width = piece.shape[1] // GRAD_CHUNKS
    ctx_in = context
    shards = []
    for c in range(GRAD_CHUNKS):
        if c >= 2:
            ctx_in, _ = lax.optimization_barrier((ctx_in, shards[c - 2]))
        weight_grad = lax.dot_general(
            ctx_in,
            piece[:, c * width:(c + 1) * width],
            (((0,), (0,)), ((), ())),
            preferred_element_type=jnp.float32,
        )
        shards.append(
            lax.psum_scatter(weight_grad.astype(jnp.bfloat16), "dp", scatter_dimension=0, tiled=True)
        )
    grad_shard = jnp.concatenate(shards, axis=1).astype(jnp.float32)
    tokens_all = tok_rows * lax.axis_size("dp")
    grad = grad_shard * (1.0 / math.sqrt(tokens_all))
    new_moment_one = 0.9 * moment_one + 0.1 * grad
    new_moment_two = 0.999 * moment_two + 0.001 * grad * grad
    first_fix = 1.0 - 0.9**10
    second_fix = 1.0 - 0.999**10
    update = (
        new_moment_one / first_fix / (jnp.sqrt(new_moment_two / second_fix) + 1e-08) + 0.1 * weight
    )
    new_weight = weight - 0.001 * update
    return (summed, d_context, new_weight, new_moment_one, new_moment_two)


def solution(mesh):
    placed = (
        P("dp", "mp"),
        P(("mp", "dp"), None),
        P(("mp", "dp"), None),
        P(("mp", "dp"), None),
        P(("dp", "mp"), None),
    )
    return jax.shard_map(
        per_device,
        mesh=mesh,
        in_specs=placed,
        out_specs=(
            P(("dp", "mp"), None),
            P("dp", "mp"),
            P(("mp", "dp"), None),
            P(("mp", "dp"), None),
            P(("mp", "dp"), None),
        ),
        check_vma=False,
    )
```

```python
import math

import jax
import jax.numpy as jnp
import numpy as np
from jax import lax
from jax.sharding import PartitionSpec as P


def ring_order(n_dp, n_mp):
    if n_dp != 32 or n_mp != 1:
        return list(range(n_dp))
    order = []
    for i, (x, y) in enumerate(((0, 0), (1, 0), (1, 1), (0, 1))):
        for z in range(4) if i % 2 == 0 else range(3, -1, -1):
            chip = (z * 2 + y) * 2 + x
            order += [chip * 2, chip * 2 + 1]
    return order


def make_per_device(order):
    n = len(order)
    position = [0] * n
    for i, d in enumerate(order):
        position[d] = i
    forward = [(order[i], order[(i + 1) % n]) for i in range(n)]
    backward = [(order[(i + 1) % n], order[i]) for i in range(n)]

    def per_device(context, weight, moment_one, moment_two, grad_out):
        weight_bf, weight = lax.optimization_barrier((weight.astype(jnp.bfloat16), weight))
        rows = weight_bf.shape[0]
        tok_rows = context.shape[0]
        piece = lax.all_gather(grad_out, "mp", axis=0, tiled=True)
        weight_grad = lax.dot_general(
            context, piece, (((0,), (0,)), ((), ())), preferred_element_type=jnp.float32
        )
        grad_shard = lax.psum_scatter(
            weight_grad.astype(jnp.bfloat16), "dp", scatter_dimension=0, tiled=True
        ).astype(jnp.float32)

        width = piece.shape[1]
        half = width // 2
        ctx_t = context.T
        order_arr = jnp.asarray(np.array(order, np.int32))
        me = jnp.asarray(np.array(position, np.int32))[lax.axis_index("dp")]
        cw = weight_bf[:, :half]
        ccw = weight_bf[:, half:]
        out_cw = jnp.zeros((tok_rows, half), jnp.float32)
        out_ccw = jnp.zeros((tok_rows, width - half), jnp.float32)
        dctx_t = jnp.zeros((ctx_t.shape[0], tok_rows), jnp.float32)
        dims_fwd = (((0,), (0,)), ((), ()))
        dims_bwd = (((1,), (1,)), ((), ()))
        def consume(step, cw, ccw, out_cw, out_ccw, dctx_t):
            src_cw = order_arr[(me - step) % n] * rows
            src_ccw = order_arr[(me + step) % n] * rows
            ctx_cw = lax.dynamic_slice_in_dim(ctx_t, src_cw, rows, 0)
            ctx_ccw = lax.dynamic_slice_in_dim(ctx_t, src_ccw, rows, 0)
            out_cw = out_cw + lax.dot_general(ctx_cw, cw, dims_fwd, preferred_element_type=jnp.float32)
            out_ccw = out_ccw + lax.dot_general(ctx_ccw, ccw, dims_fwd, preferred_element_type=jnp.float32)
            part_cw = lax.dot_general(cw, piece[:, :half], dims_bwd, preferred_element_type=jnp.float32)
            dctx_t = lax.dynamic_update_slice_in_dim(
                dctx_t, lax.dynamic_slice_in_dim(dctx_t, src_cw, rows, 0) + part_cw, src_cw, 0
            )
            part_ccw = lax.dot_general(ccw, piece[:, half:], dims_bwd, preferred_element_type=jnp.float32)
            dctx_t = lax.dynamic_update_slice_in_dim(
                dctx_t, lax.dynamic_slice_in_dim(dctx_t, src_ccw, rows, 0) + part_ccw, src_ccw, 0
            )
            return out_cw, out_ccw, dctx_t

        def ring_step(step, carry):
            cw, ccw, out_cw, out_ccw, dctx_t = carry
            cw_next = lax.ppermute(cw, "dp", forward)
            ccw_next = lax.ppermute(ccw, "dp", backward)
            out_cw, out_ccw, dctx_t = consume(step, cw, ccw, out_cw, out_ccw, dctx_t)
            return cw_next, ccw_next, out_cw, out_ccw, dctx_t

        cw, ccw, out_cw, out_ccw, dctx_t = lax.fori_loop(
            0, n - 1, ring_step, (cw, ccw, out_cw, out_ccw, dctx_t)
        )
        out_cw, out_ccw, dctx_t = consume(n - 1, cw, ccw, out_cw, out_ccw, dctx_t)
        partials = jnp.concatenate([out_cw, out_ccw], axis=1)
        summed = lax.psum_scatter(partials.astype(jnp.bfloat16), "mp", scatter_dimension=0, tiled=True)
        d_context = dctx_t.T.astype(jnp.bfloat16)

        tokens_all = tok_rows * lax.axis_size("dp")
        grad = grad_shard * (1.0 / math.sqrt(tokens_all))
        new_moment_one = 0.9 * moment_one + 0.1 * grad
        new_moment_two = 0.999 * moment_two + 0.001 * grad * grad
        first_fix = 1.0 - 0.9**10
        second_fix = 1.0 - 0.999**10
        update = (
            new_moment_one / first_fix / (jnp.sqrt(new_moment_two / second_fix) + 1e-08) + 0.1 * weight
        )
        new_weight = weight - 0.001 * update
        return (summed, d_context, new_weight, new_moment_one, new_moment_two)

    return per_device


def solution(mesh):
    placed = (
        P("dp", "mp"),
        P(("mp", "dp"), None),
        P(("mp", "dp"), None),
        P(("mp", "dp"), None),
        P(("dp", "mp"), None),
    )
    order = ring_order(mesh.shape["dp"], mesh.shape["mp"])
    return jax.shard_map(
        make_per_device(order),
        mesh=mesh,
        in_specs=placed,
        out_specs=(
            P(("dp", "mp"), None),
            P("dp", "mp"),
            P(("mp", "dp"), None),
            P(("mp", "dp"), None),
            P(("mp", "dp"), None),
        ),
        check_vma=False,
    )
```

```python
import math

import jax
import jax.numpy as jnp
import numpy as np
from jax import lax
from jax.sharding import PartitionSpec as P


def ring_order(n_dp, n_mp):
    if n_dp != 32 or n_mp != 1:
        return list(range(n_dp))
    order = []
    for i, (x, y) in enumerate(((0, 0), (1, 0), (1, 1), (0, 1))):
        for z in range(4) if i % 2 == 0 else range(3, -1, -1):
            chip = (z * 2 + y) * 2 + x
            order += [chip * 2, chip * 2 + 1]
    return order


def make_per_device(order):
    n = len(order)
    position = [0] * n
    for i, d in enumerate(order):
        position[d] = i
    forward = [(order[i], order[(i + 1) % n]) for i in range(n)]
    backward = [(order[(i + 1) % n], order[i]) for i in range(n)]

    def per_device(context, weight, moment_one, moment_two, grad_out):
        weight_bf, weight = lax.optimization_barrier((weight.astype(jnp.bfloat16), weight))
        rows = weight_bf.shape[0]
        tok_rows = context.shape[0]
        piece = lax.all_gather(grad_out, "mp", axis=0, tiled=True)
        weight_grad = lax.dot_general(
            context, piece, (((0,), (0,)), ((), ())), preferred_element_type=jnp.float32
        )
        grad_shard = lax.psum_scatter(
            weight_grad.astype(jnp.bfloat16), "dp", scatter_dimension=0, tiled=True
        ).astype(jnp.float32)

        half = rows // 2
        ctx_t = context.T
        order_arr = jnp.asarray(np.array(order, np.int32))
        me = jnp.asarray(np.array(position, np.int32))[lax.axis_index("dp")]
        cw = weight_bf[:half]
        ccw = weight_bf[half:]
        out = jnp.zeros((tok_rows, piece.shape[1]), jnp.float32)
        dctx_t = jnp.zeros((ctx_t.shape[0], tok_rows), jnp.bfloat16)
        dims_fwd = (((0,), (0,)), ((), ()))
        dims_bwd = (((1,), (1,)), ((), ()))

        def consume(step, cw, ccw, out, dctx_t):
            src_cw = order_arr[(me - step) % n] * rows
            src_ccw = order_arr[(me + step) % n] * rows + half
            ctx_blk = jnp.concatenate(
                [
                    lax.dynamic_slice_in_dim(ctx_t, src_cw, half, 0),
                    lax.dynamic_slice_in_dim(ctx_t, src_ccw, rows - half, 0),
                ],
                axis=0,
            )
            w_blk = jnp.concatenate([cw, ccw], axis=0)
            out = out + lax.dot_general(ctx_blk, w_blk, dims_fwd, preferred_element_type=jnp.float32)
            part_cw = lax.dot_general(cw, piece, dims_bwd, preferred_element_type=jnp.float32)
            dctx_t = lax.dynamic_update_slice_in_dim(dctx_t, part_cw.astype(jnp.bfloat16), src_cw, 0)
            part_ccw = lax.dot_general(ccw, piece, dims_bwd, preferred_element_type=jnp.float32)
            dctx_t = lax.dynamic_update_slice_in_dim(dctx_t, part_ccw.astype(jnp.bfloat16), src_ccw, 0)
            return out, dctx_t

        def ring_step(step, carry):
            cw, ccw, out, dctx_t = carry
            cw_next = lax.ppermute(cw, "dp", forward)
            ccw_next = lax.ppermute(ccw, "dp", backward)
            out, dctx_t = consume(step, cw, ccw, out, dctx_t)
            return cw_next, ccw_next, out, dctx_t

        cw, ccw, out, dctx_t = lax.fori_loop(0, n - 1, ring_step, (cw, ccw, out, dctx_t))
        out, dctx_t = consume(n - 1, cw, ccw, out, dctx_t)
        summed = lax.psum_scatter(out.astype(jnp.bfloat16), "mp", scatter_dimension=0, tiled=True)
        d_context = dctx_t.T

        tokens_all = tok_rows * lax.axis_size("dp")
        grad = grad_shard * (1.0 / math.sqrt(tokens_all))
        new_moment_one = 0.9 * moment_one + 0.1 * grad
        new_moment_two = 0.999 * moment_two + 0.001 * grad * grad
        first_fix = 1.0 - 0.9**10
        second_fix = 1.0 - 0.999**10
        update = (
            new_moment_one / first_fix / (jnp.sqrt(new_moment_two / second_fix) + 1e-08) + 0.1 * weight
        )
        new_weight = weight - 0.001 * update
        return (summed, d_context, new_weight, new_moment_one, new_moment_two)

    return per_device


def solution(mesh):
    placed = (
        P("dp", "mp"),
        P(("mp", "dp"), None),
        P(("mp", "dp"), None),
        P(("mp", "dp"), None),
        P(("dp", "mp"), None),
    )
    order = ring_order(mesh.shape["dp"], mesh.shape["mp"])
    return jax.shard_map(
        make_per_device(order),
        mesh=mesh,
        in_specs=placed,
        out_specs=(
            P(("dp", "mp"), None),
            P("dp", "mp"),
            P(("mp", "dp"), None),
            P(("mp", "dp"), None),
            P(("mp", "dp"), None),
        ),
        check_vma=False,
    )
```

```python
import math

import jax
import jax.numpy as jnp
from jax import lax
from jax.sharding import Mesh
from jax.sharding import PartitionSpec as P

DP = ("chip", "core")


def per_device(context, weight, moment_one, moment_two, grad_out):
    rows = weight.shape[0]
    tok_rows, local_cols = context.shape
    chips = lax.axis_size("chip")
    weight_bf = weight.astype(jnp.bfloat16)
    piece = lax.all_gather(grad_out, "mp", axis=0, tiled=True)
    width = piece.shape[1]
    swap = [(0, 1), (1, 0)]
    ctx_split = context.reshape(tok_rows, chips, 2, rows)
    me = lax.axis_index("core")
    ctx_own = jnp.where(me == 0, ctx_split[:, :, 0], ctx_split[:, :, 1]).reshape(tok_rows, chips * rows)
    ctx_other = jnp.where(me == 0, ctx_split[:, :, 1], ctx_split[:, :, 0]).reshape(tok_rows, chips * rows)
    dims_wgrad = (((0,), (0,)), ((), ()))

    grad_for_other = lax.dot_general(
        ctx_other, piece, dims_wgrad, preferred_element_type=jnp.float32
    ).astype(jnp.bfloat16)
    grad_from_other = lax.ppermute(grad_for_other, "core", swap)

    own_half = lax.all_gather(weight_bf, "chip", axis=0, tiled=True)
    grad_mine = lax.dot_general(ctx_own, piece, dims_wgrad, preferred_element_type=jnp.float32)
    chip_grad = (grad_mine + grad_from_other.astype(jnp.float32)).astype(jnp.bfloat16)
    chip_grad, own_half = lax.optimization_barrier((chip_grad, own_half))
    grad_shard = lax.psum_scatter(chip_grad, "chip", scatter_dimension=0, tiled=True).astype(jnp.float32)

    other_half = lax.ppermute(own_half, "core", swap)
    out = jnp.dot(ctx_own, own_half, preferred_element_type=jnp.float32)
    d_own = lax.dot_general(piece, own_half, (((1,), (1,)), ((), ())), preferred_element_type=jnp.float32)
    out = out + jnp.dot(ctx_other, other_half, preferred_element_type=jnp.float32)
    d_other = lax.dot_general(
        piece, other_half, (((1,), (1,)), ((), ())), preferred_element_type=jnp.float32
    )
    summed = lax.psum_scatter(out.astype(jnp.bfloat16), "mp", scatter_dimension=0, tiled=True)
    d_own = d_own.astype(jnp.bfloat16).reshape(tok_rows, chips, rows)
    d_other = d_other.astype(jnp.bfloat16).reshape(tok_rows, chips, rows)
    first = jnp.where(me == 0, d_own, d_other)
    second = jnp.where(me == 0, d_other, d_own)
    d_context = jnp.stack([first, second], axis=2).reshape(tok_rows, local_cols)

    tokens_all = tok_rows * chips * 2
    grad = grad_shard * (1.0 / math.sqrt(tokens_all))
    new_moment_one = 0.9 * moment_one + 0.1 * grad
    new_moment_two = 0.999 * moment_two + 0.001 * grad * grad
    first_fix = 1.0 - 0.9**10
    second_fix = 1.0 - 0.999**10
    update = (
        new_moment_one / first_fix / (jnp.sqrt(new_moment_two / second_fix) + 1e-08) + 0.1 * weight
    )
    new_weight = weight - 0.001 * update
    return (summed, d_context, new_weight, new_moment_one, new_moment_two)


def solution(mesh):
    names = mesh.axis_names
    devices = mesh.devices.transpose([names.index("dp"), names.index("mp")])
    n_dp, n_mp = devices.shape
    split = Mesh(devices.reshape(n_dp // 2, 2, n_mp), ("chip", "core", "mp"))
    placed = (
        P(DP, "mp"),
        P(("mp",) + DP, None),
        P(("mp",) + DP, None),
        P(("mp",) + DP, None),
        P(DP + ("mp",), None),
    )
    return jax.shard_map(
        per_device,
        mesh=split,
        in_specs=placed,
        out_specs=(
            P(DP + ("mp",), None),
            P(DP, "mp"),
            P(("mp",) + DP, None),
            P(("mp",) + DP, None),
            P(("mp",) + DP, None),
        ),
        check_vma=False,
    )
```

```python
import math

import jax
import jax.numpy as jnp
import numpy as np
from jax import lax
from jax.sharding import Mesh
from jax.sharding import PartitionSpec as P

DP = ("chip", "core")


def chip_cycle(n):
    if n != 16:
        return list(range(n))
    order = []
    for i, (x, y) in enumerate(((0, 0), (1, 0), (1, 1), (0, 1))):
        for z in range(4) if i % 2 == 0 else range(3, -1, -1):
            order.append((z * 2 + y) * 2 + x)
    return order


def per_device(context, weight, moment_one, moment_two, grad_out):
    rows = weight.shape[0]
    tok_rows, local_cols = context.shape
    chips = lax.axis_size("chip")
    weight_bf = weight.astype(jnp.bfloat16)
    piece = lax.all_gather(grad_out, "mp", axis=0, tiled=True)
    width = piece.shape[1]
    swap = [(0, 1), (1, 0)]
    ctx_split = context.reshape(tok_rows, chips, 2, rows)
    me = lax.axis_index("core")
    ctx_own = jnp.where(me == 0, ctx_split[:, :, 0], ctx_split[:, :, 1]).reshape(tok_rows, chips * rows)
    ctx_other = jnp.where(me == 0, ctx_split[:, :, 1], ctx_split[:, :, 0]).reshape(tok_rows, chips * rows)
    dims_wgrad = (((0,), (0,)), ((), ()))

    grad_for_other = lax.dot_general(
        ctx_other, piece, dims_wgrad, preferred_element_type=jnp.float32
    ).astype(jnp.bfloat16)
    grad_from_other = lax.ppermute(grad_for_other, "core", swap)

    grad_mine = lax.dot_general(ctx_own, piece, dims_wgrad, preferred_element_type=jnp.float32)
    chip_grad = (grad_mine + grad_from_other.astype(jnp.float32)).astype(jnp.bfloat16)
    weight_bf, chip_grad = lax.optimization_barrier((weight_bf, chip_grad))
    full_weight = lax.all_gather(weight_bf, DP, axis=0, tiled=True)

    n = chips
    order = chip_cycle(n)
    position = [0] * n
    for i, c in enumerate(order):
        position[c] = i
    forward = [(order[i], order[(i + 1) % n]) for i in range(n)]
    backward = [(order[(i + 1) % n], order[i]) for i in range(n)]
    order_arr = jnp.asarray(np.array(order, np.int32))
    pos = jnp.asarray(np.array(position, np.int32))[lax.axis_index("chip")]
    half = width // 2

    def own_block(block):
        return lax.dynamic_slice_in_dim(chip_grad, block * rows, rows, 0).astype(jnp.float32)

    def ring_step(step, carry):
        send_cw, send_ccw = carry
        recv_cw = lax.ppermute(send_cw, "chip", forward)
        recv_ccw = lax.ppermute(send_ccw, "chip", backward)
        mine_cw = own_block(order_arr[(pos - step - 2) % n])[:, :half]
        mine_ccw = own_block(order_arr[(pos + step + 2) % n])[:, half:]
        return (
            (recv_cw.astype(jnp.float32) + mine_cw).astype(jnp.bfloat16),
            (recv_ccw.astype(jnp.float32) + mine_ccw).astype(jnp.bfloat16),
        )

    start_cw = own_block(order_arr[(pos - 1) % n])[:, :half].astype(jnp.bfloat16)
    start_ccw = own_block(order_arr[(pos + 1) % n])[:, half:].astype(jnp.bfloat16)
    done_cw, done_ccw = lax.fori_loop(0, n - 1, ring_step, (start_cw, start_ccw))
    grad_shard = jnp.concatenate([done_cw, done_ccw], axis=1).astype(jnp.float32)
    full_weight, grad_shard = lax.optimization_barrier((full_weight, grad_shard))

    out = jnp.dot(context, full_weight, preferred_element_type=jnp.float32)
    summed = lax.psum_scatter(out.astype(jnp.bfloat16), "mp", scatter_dimension=0, tiled=True)
    d_context = lax.dot_general(
        piece, full_weight, (((1,), (1,)), ((), ())), preferred_element_type=jnp.float32
    ).astype(jnp.bfloat16)

    tokens_all = tok_rows * chips * 2
    grad = grad_shard * (1.0 / math.sqrt(tokens_all))
    new_moment_one = 0.9 * moment_one + 0.1 * grad
    new_moment_two = 0.999 * moment_two + 0.001 * grad * grad
    first_fix = 1.0 - 0.9**10
    second_fix = 1.0 - 0.999**10
    update = (
        new_moment_one / first_fix / (jnp.sqrt(new_moment_two / second_fix) + 1e-08) + 0.1 * weight
    )
    new_weight = weight - 0.001 * update
    return (summed, d_context, new_weight, new_moment_one, new_moment_two)


def solution(mesh):
    names = mesh.axis_names
    devices = mesh.devices.transpose([names.index("dp"), names.index("mp")])
    n_dp, n_mp = devices.shape
    split = Mesh(devices.reshape(n_dp // 2, 2, n_mp), ("chip", "core", "mp"))
    placed = (
        P(DP, "mp"),
        P(("mp",) + DP, None),
        P(("mp",) + DP, None),
        P(("mp",) + DP, None),
        P(DP + ("mp",), None),
    )
    return jax.shard_map(
        per_device,
        mesh=split,
        in_specs=placed,
        out_specs=(
            P(DP + ("mp",), None),
            P(DP, "mp"),
            P(("mp",) + DP, None),
            P(("mp",) + DP, None),
            P(("mp",) + DP, None),
        ),
        check_vma=False,
    )
```

```python
import math

import jax
import jax.numpy as jnp
import numpy as np
from jax import lax
from jax.sharding import Mesh
from jax.sharding import PartitionSpec as P

DP = ("chip", "core")


def chip_cycle(n):
    if n != 16:
        return list(range(n))
    order = []
    for i, (x, y) in enumerate(((0, 0), (1, 0), (1, 1), (0, 1))):
        for z in range(4) if i % 2 == 0 else range(3, -1, -1):
            order.append((z * 2 + y) * 2 + x)
    return order


def per_device(context, weight, moment_one, moment_two, grad_out):
    rows = weight.shape[0]
    tok_rows, local_cols = context.shape
    chips = lax.axis_size("chip")
    weight_bf = weight.astype(jnp.bfloat16)
    piece = lax.all_gather(grad_out, "mp", axis=0, tiled=True)
    width = piece.shape[1]
    swap = [(0, 1), (1, 0)]
    ctx_split = context.reshape(tok_rows, chips, 2, rows)
    me = lax.axis_index("core")
    ctx_own = jnp.where(me == 0, ctx_split[:, :, 0], ctx_split[:, :, 1]).reshape(tok_rows, chips * rows)
    ctx_other = jnp.where(me == 0, ctx_split[:, :, 1], ctx_split[:, :, 0]).reshape(tok_rows, chips * rows)
    dims_wgrad = (((0,), (0,)), ((), ()))

    full_weight = lax.all_gather(weight_bf, DP, axis=0, tiled=True)
    quarter = chips * rows // 4
    sums = []
    for q in range(4):
        cols = slice(q * quarter, (q + 1) * quarter)
        ctx_q = ctx_other[:, cols]
        if sums:
            ctx_q, _ = lax.optimization_barrier((ctx_q, sums[-1]))
        grad_for_other = lax.dot_general(
            ctx_q, piece, dims_wgrad, preferred_element_type=jnp.float32
        ).astype(jnp.bfloat16)
        grad_from_other = lax.ppermute(grad_for_other, "core", swap)
        grad_mine = lax.dot_general(ctx_own[:, cols], piece, dims_wgrad, preferred_element_type=jnp.float32)
        sums.append((grad_mine + grad_from_other.astype(jnp.float32)).astype(jnp.bfloat16))

    n = chips
    order = chip_cycle(n)
    position = [0] * n
    for i, c in enumerate(order):
        position[c] = i
    forward = [(order[i], order[(i + 1) % n]) for i in range(n)]
    backward = [(order[(i + 1) % n], order[i]) for i in range(n)]
    order_arr = jnp.asarray(np.array(order, np.int32))
    pos = jnp.asarray(np.array(position, np.int32))[lax.axis_index("chip")]
    half = width // 2

    per_quarter = quarter // rows

    def own_block(block):
        within = (block % per_quarter) * rows
        which = block // per_quarter
        picked = lax.dynamic_slice_in_dim(sums[0], within, rows, 0)
        for q in range(1, 4):
            picked = jnp.where(which == q, lax.dynamic_slice_in_dim(sums[q], within, rows, 0), picked)
        return picked.astype(jnp.float32)

    n_pieces = 3
    out_cols = width // n_pieces
    d_rows = local_cols // n_pieces

    def product(j, w):
        if j < n_pieces:
            return jnp.dot(
                context, w[:, j * out_cols:(j + 1) * out_cols], preferred_element_type=jnp.float32
            ).astype(jnp.bfloat16)
        k = j - n_pieces
        return lax.dot_general(
            piece, w[k * d_rows:(k + 1) * d_rows], (((1,), (1,)), ((), ())),
            preferred_element_type=jnp.float32,
        ).astype(jnp.bfloat16)

    send_cw = own_block(order_arr[(pos - 1) % n])[:, :half].astype(jnp.bfloat16)
    send_ccw = own_block(order_arr[(pos + 1) % n])[:, half:].astype(jnp.bfloat16)
    products = []
    first_piece = max(0, n - 1 - 2 * n_pieces)
    for step in range(n - 1):
        recv_cw = lax.ppermute(send_cw, "chip", forward)
        recv_ccw = lax.ppermute(send_ccw, "chip", backward)
        j = step - first_piece
        if 0 <= j < 2 * n_pieces:
            w_now, _ = lax.optimization_barrier((full_weight, send_cw))
            products.append(product(j, w_now))
        mine_cw = own_block(order_arr[(pos - step - 2) % n])[:, :half]
        mine_ccw = own_block(order_arr[(pos + step + 2) % n])[:, half:]
        send_cw = (recv_cw.astype(jnp.float32) + mine_cw).astype(jnp.bfloat16)
        send_ccw = (recv_ccw.astype(jnp.float32) + mine_ccw).astype(jnp.bfloat16)
        if 0 <= j < 2 * n_pieces:
            send_cw, send_ccw, products[-1] = lax.optimization_barrier((send_cw, send_ccw, products[-1]))
    for j in range(len(products), 2 * n_pieces):
        products.append(product(j, full_weight))
    grad_shard = jnp.concatenate([send_cw, send_ccw], axis=1).astype(jnp.float32)
    out = jnp.concatenate(products[:n_pieces], axis=1)
    summed = lax.psum_scatter(out, "mp", scatter_dimension=0, tiled=True)
    d_context = jnp.concatenate(products[n_pieces:], axis=1)

    tokens_all = tok_rows * chips * 2
    grad = grad_shard * (1.0 / math.sqrt(tokens_all))
    new_moment_one = 0.9 * moment_one + 0.1 * grad
    new_moment_two = 0.999 * moment_two + 0.001 * grad * grad
    first_fix = 1.0 - 0.9**10
    second_fix = 1.0 - 0.999**10
    update = (
        new_moment_one / first_fix / (jnp.sqrt(new_moment_two / second_fix) + 1e-08) + 0.1 * weight
    )
    new_weight = weight - 0.001 * update
    return (summed, d_context, new_weight, new_moment_one, new_moment_two)


def solution(mesh):
    names = mesh.axis_names
    devices = mesh.devices.transpose([names.index("dp"), names.index("mp")])
    n_dp, n_mp = devices.shape
    split = Mesh(devices.reshape(n_dp // 2, 2, n_mp), ("chip", "core", "mp"))
    placed = (
        P(DP, "mp"),
        P(("mp",) + DP, None),
        P(("mp",) + DP, None),
        P(("mp",) + DP, None),
        P(DP + ("mp",), None),
    )
    return jax.shard_map(
        per_device,
        mesh=split,
        in_specs=placed,
        out_specs=(
            P(DP + ("mp",), None),
            P(DP, "mp"),
            P(("mp",) + DP, None),
            P(("mp",) + DP, None),
            P(("mp",) + DP, None),
        ),
        check_vma=False,
    )
```

```python
import math

import jax
import jax.numpy as jnp
import numpy as np
from jax import lax
from jax.sharding import Mesh
from jax.sharding import PartitionSpec as P

DP = ("chip", "core")


def chip_cycle(n):
    if n != 16:
        return list(range(n))
    order = []
    for i, (x, y) in enumerate(((0, 0), (1, 0), (1, 1), (0, 1))):
        for z in range(4) if i % 2 == 0 else range(3, -1, -1):
            order.append((z * 2 + y) * 2 + x)
    return order


def per_device(context, weight, moment_one, moment_two, grad_out):
    rows = weight.shape[0]
    tok_rows, local_cols = context.shape
    chips = lax.axis_size("chip")
    weight_bf = weight.astype(jnp.bfloat16)
    piece = lax.all_gather(grad_out, "mp", axis=0, tiled=True)
    width = piece.shape[1]
    swap = [(0, 1), (1, 0)]
    ctx_split = context.reshape(tok_rows, chips, 2, rows)
    me = lax.axis_index("core")
    ctx_own = jnp.where(me == 0, ctx_split[:, :, 0], ctx_split[:, :, 1]).reshape(tok_rows, chips * rows)
    ctx_other = jnp.where(me == 0, ctx_split[:, :, 1], ctx_split[:, :, 0]).reshape(tok_rows, chips * rows)
    dims_wgrad = (((0,), (0,)), ((), ()))

    full_weight = lax.all_gather(weight_bf, DP, axis=0, tiled=True)
    quarter = chips * rows // 4
    sums = []
    for q in range(4):
        cols = slice(q * quarter, (q + 1) * quarter)
        ctx_q = ctx_other[:, cols]
        if sums:
            ctx_q, _ = lax.optimization_barrier((ctx_q, sums[-1]))
        grad_for_other = lax.dot_general(
            ctx_q, piece, dims_wgrad, preferred_element_type=jnp.float32
        ).astype(jnp.bfloat16)
        grad_from_other = lax.ppermute(grad_for_other, "core", swap)
        grad_mine = lax.dot_general(ctx_own[:, cols], piece, dims_wgrad, preferred_element_type=jnp.float32)
        sums.append((grad_mine + grad_from_other.astype(jnp.float32)).astype(jnp.bfloat16))

    n = chips
    order = chip_cycle(n)
    position = [0] * n
    for i, c in enumerate(order):
        position[c] = i
    forward = [(order[i], order[(i + 1) % n]) for i in range(n)]
    backward = [(order[(i + 1) % n], order[i]) for i in range(n)]
    order_arr = jnp.asarray(np.array(order, np.int32))
    pos = jnp.asarray(np.array(position, np.int32))[lax.axis_index("chip")]
    half = width // 2

    per_quarter = quarter // rows

    def own_block(block):
        within = (block % per_quarter) * rows
        which = block // per_quarter
        picked = lax.dynamic_slice_in_dim(sums[0], within, rows, 0)
        for q in range(1, 4):
            picked = jnp.where(which == q, lax.dynamic_slice_in_dim(sums[q], within, rows, 0), picked)
        return picked.astype(jnp.float32)

    n_pieces = 3
    out_cols = width // n_pieces
    d_rows = local_cols // n_pieces

    def product(j, w):
        if j < n_pieces:
            return jnp.dot(
                context, w[:, j * out_cols:(j + 1) * out_cols], preferred_element_type=jnp.float32
            ).astype(jnp.bfloat16)
        k = j - n_pieces
        return lax.dot_general(
            piece, w[k * d_rows:(k + 1) * d_rows], (((1,), (1,)), ((), ())),
            preferred_element_type=jnp.float32,
        ).astype(jnp.bfloat16)

    send_cw = own_block(order_arr[(pos - 1) % n])[:, :half].astype(jnp.bfloat16)
    send_ccw = own_block(order_arr[(pos + 1) % n])[:, half:].astype(jnp.bfloat16)
    products = []
    first_piece = max(0, n - 3 - 2 * n_pieces)
    for step in range(n - 1):
        recv_cw = lax.ppermute(send_cw, "chip", forward)
        recv_ccw = lax.ppermute(send_ccw, "chip", backward)
        j = step - first_piece
        if 0 <= j < 2 * n_pieces:
            w_now, _ = lax.optimization_barrier((full_weight, send_cw))
            products.append(product(j, w_now))
        mine_cw = own_block(order_arr[(pos - step - 2) % n])[:, :half]
        mine_ccw = own_block(order_arr[(pos + step + 2) % n])[:, half:]
        send_cw = (recv_cw.astype(jnp.float32) + mine_cw).astype(jnp.bfloat16)
        send_ccw = (recv_ccw.astype(jnp.float32) + mine_ccw).astype(jnp.bfloat16)
        if 0 <= j < 2 * n_pieces:
            send_cw, send_ccw, products[-1] = lax.optimization_barrier((send_cw, send_ccw, products[-1]))
    for j in range(len(products), 2 * n_pieces):
        products.append(product(j, full_weight))
    grad_shard = jnp.concatenate([send_cw, send_ccw], axis=1).astype(jnp.float32)
    out = jnp.concatenate(products[:n_pieces], axis=1)
    summed = lax.psum_scatter(out, "mp", scatter_dimension=0, tiled=True)
    d_context = jnp.concatenate(products[n_pieces:], axis=1)

    tokens_all = tok_rows * chips * 2
    grad = grad_shard * (1.0 / math.sqrt(tokens_all))
    new_moment_one = 0.9 * moment_one + 0.1 * grad
    new_moment_two = 0.999 * moment_two + 0.001 * grad * grad
    first_fix = 1.0 - 0.9**10
    second_fix = 1.0 - 0.999**10
    update = (
        new_moment_one / first_fix / (jnp.sqrt(new_moment_two / second_fix) + 1e-08) + 0.1 * weight
    )
    new_weight = weight - 0.001 * update
    return (summed, d_context, new_weight, new_moment_one, new_moment_two)


def solution(mesh):
    names = mesh.axis_names
    devices = mesh.devices.transpose([names.index("dp"), names.index("mp")])
    n_dp, n_mp = devices.shape
    split = Mesh(devices.reshape(n_dp // 2, 2, n_mp), ("chip", "core", "mp"))
    placed = (
        P(DP, "mp"),
        P(("mp",) + DP, None),
        P(("mp",) + DP, None),
        P(("mp",) + DP, None),
        P(DP + ("mp",), None),
    )
    return jax.shard_map(
        per_device,
        mesh=split,
        in_specs=placed,
        out_specs=(
            P(DP + ("mp",), None),
            P(DP, "mp"),
            P(("mp",) + DP, None),
            P(("mp",) + DP, None),
            P(("mp",) + DP, None),
        ),
        check_vma=False,
    )
```

```python
import math

import jax
import jax.numpy as jnp
import numpy as np
from jax import lax
from jax.sharding import Mesh
from jax.sharding import PartitionSpec as P

DP = ("chip", "core")


def chip_cycle(n):
    if n != 16:
        return list(range(n))
    order = []
    for i, (x, y) in enumerate(((0, 0), (1, 0), (1, 1), (0, 1))):
        for z in range(4) if i % 2 == 0 else range(3, -1, -1):
            order.append((z * 2 + y) * 2 + x)
    return order


def per_device(context, weight, moment_one, moment_two, grad_out):
    rows = weight.shape[0]
    tok_rows, local_cols = context.shape
    chips = lax.axis_size("chip")
    weight_bf = weight.astype(jnp.bfloat16)
    piece = lax.all_gather(grad_out, "mp", axis=0, tiled=True)
    width = piece.shape[1]
    swap = [(0, 1), (1, 0)]
    ctx_split = context.reshape(tok_rows, chips, 2, rows)
    me = lax.axis_index("core")
    ctx_own = jnp.where(me == 0, ctx_split[:, :, 0], ctx_split[:, :, 1]).reshape(tok_rows, chips * rows)
    ctx_other = jnp.where(me == 0, ctx_split[:, :, 1], ctx_split[:, :, 0]).reshape(tok_rows, chips * rows)
    dims_wgrad = (((0,), (0,)), ((), ()))

    full_weight = lax.all_gather(weight_bf, DP, axis=0, tiled=True)
    quarter = width // 4
    sums = []
    for q in range(4):
        piece_q = piece[:, q * quarter:(q + 1) * quarter]
        if sums:
            piece_q, _ = lax.optimization_barrier((piece_q, sums[-1]))
        grad_for_other = lax.dot_general(
            ctx_other, piece_q, dims_wgrad, preferred_element_type=jnp.float32
        ).astype(jnp.bfloat16)
        grad_from_other = lax.ppermute(grad_for_other, "core", swap)
        grad_mine = lax.dot_general(ctx_own, piece_q, dims_wgrad, preferred_element_type=jnp.float32)
        sums.append((grad_mine + grad_from_other.astype(jnp.float32)).astype(jnp.bfloat16))

    n = chips
    order = chip_cycle(n)
    position = [0] * n
    for i, c in enumerate(order):
        position[c] = i
    forward = [(order[i], order[(i + 1) % n]) for i in range(n)]
    backward = [(order[(i + 1) % n], order[i]) for i in range(n)]
    order_arr = jnp.asarray(np.array(order, np.int32))
    pos = jnp.asarray(np.array(position, np.int32))[lax.axis_index("chip")]
    half = width // 2

    def own_block(block, first):
        return jnp.concatenate(
            [lax.dynamic_slice_in_dim(sums[q], block * rows, rows, 0) for q in (first, first + 1)], axis=1
        ).astype(jnp.float32)

    n_pieces = 3
    out_cols = width // n_pieces
    d_rows = local_cols // n_pieces

    def product(j, w):
        if j < n_pieces:
            return jnp.dot(
                context, w[:, j * out_cols:(j + 1) * out_cols], preferred_element_type=jnp.float32
            ).astype(jnp.bfloat16)
        k = j - n_pieces
        return lax.dot_general(
            piece, w[k * d_rows:(k + 1) * d_rows], (((1,), (1,)), ((), ())),
            preferred_element_type=jnp.float32,
        ).astype(jnp.bfloat16)

    send_cw = own_block(order_arr[(pos - 1) % n], 0).astype(jnp.bfloat16)
    send_ccw = own_block(order_arr[(pos + 1) % n], 2).astype(jnp.bfloat16)
    products = []
    first_piece = max(0, n - 3 - 2 * n_pieces)
    for step in range(n - 1):
        recv_cw = lax.ppermute(send_cw, "chip", forward)
        recv_ccw = lax.ppermute(send_ccw, "chip", backward)
        j = step - first_piece
        if 0 <= j < 2 * n_pieces:
            w_now, _ = lax.optimization_barrier((full_weight, send_cw))
            products.append(product(j, w_now))
        mine_cw = own_block(order_arr[(pos - step - 2) % n], 0)
        mine_ccw = own_block(order_arr[(pos + step + 2) % n], 2)
        send_cw = (recv_cw.astype(jnp.float32) + mine_cw).astype(jnp.bfloat16)
        send_ccw = (recv_ccw.astype(jnp.float32) + mine_ccw).astype(jnp.bfloat16)
        if 0 <= j < 2 * n_pieces:
            send_cw, send_ccw, products[-1] = lax.optimization_barrier((send_cw, send_ccw, products[-1]))
    for j in range(len(products), 2 * n_pieces):
        products.append(product(j, full_weight))
    grad_shard = jnp.concatenate([send_cw, send_ccw], axis=1).astype(jnp.float32)
    out = jnp.concatenate(products[:n_pieces], axis=1)
    summed = lax.psum_scatter(out, "mp", scatter_dimension=0, tiled=True)
    d_context = jnp.concatenate(products[n_pieces:], axis=1)

    tokens_all = tok_rows * chips * 2
    grad = grad_shard * (1.0 / math.sqrt(tokens_all))
    new_moment_one = 0.9 * moment_one + 0.1 * grad
    new_moment_two = 0.999 * moment_two + 0.001 * grad * grad
    first_fix = 1.0 - 0.9**10
    second_fix = 1.0 - 0.999**10
    update = (
        new_moment_one / first_fix / (jnp.sqrt(new_moment_two / second_fix) + 1e-08) + 0.1 * weight
    )
    new_weight = weight - 0.001 * update
    return (summed, d_context, new_weight, new_moment_one, new_moment_two)


def solution(mesh):
    names = mesh.axis_names
    devices = mesh.devices.transpose([names.index("dp"), names.index("mp")])
    n_dp, n_mp = devices.shape
    split = Mesh(devices.reshape(n_dp // 2, 2, n_mp), ("chip", "core", "mp"))
    placed = (
        P(DP, "mp"),
        P(("mp",) + DP, None),
        P(("mp",) + DP, None),
        P(("mp",) + DP, None),
        P(DP + ("mp",), None),
    )
    return jax.shard_map(
        per_device,
        mesh=split,
        in_specs=placed,
        out_specs=(
            P(DP + ("mp",), None),
            P(DP, "mp"),
            P(("mp",) + DP, None),
            P(("mp",) + DP, None),
            P(("mp",) + DP, None),
        ),
        check_vma=False,
    )
```

```python
import math

import jax
import jax.numpy as jnp
import numpy as np
from jax import lax
from jax.sharding import Mesh
from jax.sharding import PartitionSpec as P

DP = ("chip", "core")


def chip_cycle(n):
    if n != 16:
        return list(range(n))
    order = []
    for i, (x, y) in enumerate(((0, 0), (1, 0), (1, 1), (0, 1))):
        for z in range(4) if i % 2 == 0 else range(3, -1, -1):
            order.append((z * 2 + y) * 2 + x)
    return order


def per_device(context, weight, moment_one, moment_two, grad_out):
    rows = weight.shape[0]
    tok_rows, local_cols = context.shape
    chips = lax.axis_size("chip")
    weight_bf = weight.astype(jnp.bfloat16)
    piece = lax.all_gather(grad_out, "mp", axis=0, tiled=True)
    width = piece.shape[1]
    swap = [(0, 1), (1, 0)]
    ctx_split = context.reshape(tok_rows, chips, 2, rows)
    me = lax.axis_index("core")
    ctx_own = jnp.where(me == 0, ctx_split[:, :, 0], ctx_split[:, :, 1]).reshape(tok_rows, chips * rows)
    ctx_other = jnp.where(me == 0, ctx_split[:, :, 1], ctx_split[:, :, 0]).reshape(tok_rows, chips * rows)
    dims_wgrad = (((0,), (0,)), ((), ()))

    full_weight = lax.all_gather(weight_bf, DP, axis=0, tiled=True)
    quarter = width // 4
    sums = []
    for q in range(4):
        piece_q = piece[:, q * quarter:(q + 1) * quarter]
        if sums:
            piece_q, _ = lax.optimization_barrier((piece_q, sums[-1]))
        grad_for_other = lax.dot_general(
            ctx_other, piece_q, dims_wgrad, preferred_element_type=jnp.float32
        ).astype(jnp.bfloat16)
        grad_from_other = lax.ppermute(grad_for_other, "core", swap)
        grad_mine = lax.dot_general(ctx_own, piece_q, dims_wgrad, preferred_element_type=jnp.float32)
        sums.append((grad_mine + grad_from_other.astype(jnp.float32)).astype(jnp.bfloat16))

    n = chips
    order = chip_cycle(n)
    position = [0] * n
    for i, c in enumerate(order):
        position[c] = i
    forward = [(order[i], order[(i + 1) % n]) for i in range(n)]
    backward = [(order[(i + 1) % n], order[i]) for i in range(n)]
    order_arr = jnp.asarray(np.array(order, np.int32))
    pos = jnp.asarray(np.array(position, np.int32))[lax.axis_index("chip")]
    half = width // 2

    def own_block(block, first):
        return jnp.concatenate(
            [lax.dynamic_slice_in_dim(sums[q], block * rows, rows, 0) for q in (first, first + 1)], axis=1
        ).astype(jnp.float32)

    n_pieces = 3
    out_cols = width // n_pieces
    d_rows = local_cols // n_pieces

    def product(j, w):
        if j < n_pieces:
            return jnp.dot(
                context, w[:, j * out_cols:(j + 1) * out_cols], preferred_element_type=jnp.float32
            ).astype(jnp.bfloat16)
        k = j - n_pieces
        return lax.dot_general(
            piece, w[k * d_rows:(k + 1) * d_rows], (((1,), (1,)), ((), ())),
            preferred_element_type=jnp.float32,
        ).astype(jnp.bfloat16)

    send_cw = own_block(order_arr[(pos - 1) % n], 0).astype(jnp.bfloat16)
    send_ccw = own_block(order_arr[(pos + 1) % n], 2).astype(jnp.bfloat16)
    products = []
    first_piece = max(0, n - 4 - 2 * n_pieces)
    for step in range(n - 1):
        recv_cw = lax.ppermute(send_cw, "chip", forward)
        recv_ccw = lax.ppermute(send_ccw, "chip", backward)
        j = step - first_piece
        if 0 <= j < 2 * n_pieces:
            w_now, _ = lax.optimization_barrier((full_weight, send_cw))
            products.append(product(j, w_now))
        mine_cw = own_block(order_arr[(pos - step - 2) % n], 0)
        mine_ccw = own_block(order_arr[(pos + step + 2) % n], 2)
        send_cw = (recv_cw.astype(jnp.float32) + mine_cw).astype(jnp.bfloat16)
        send_ccw = (recv_ccw.astype(jnp.float32) + mine_ccw).astype(jnp.bfloat16)
        if 0 <= j < 2 * n_pieces:
            send_cw, send_ccw, products[-1] = lax.optimization_barrier((send_cw, send_ccw, products[-1]))
    for j in range(len(products), 2 * n_pieces):
        products.append(product(j, full_weight))
    grad_shard = jnp.concatenate([send_cw, send_ccw], axis=1).astype(jnp.float32)
    out = jnp.concatenate(products[:n_pieces], axis=1)
    summed = lax.psum_scatter(out, "mp", scatter_dimension=0, tiled=True)
    d_context = jnp.concatenate(products[n_pieces:], axis=1)

    tokens_all = tok_rows * chips * 2
    grad = grad_shard * (1.0 / math.sqrt(tokens_all))
    new_moment_one = 0.9 * moment_one + 0.1 * grad
    new_moment_two = 0.999 * moment_two + 0.001 * grad * grad
    first_fix = 1.0 - 0.9**10
    second_fix = 1.0 - 0.999**10
    update = (
        new_moment_one / first_fix / (jnp.sqrt(new_moment_two / second_fix) + 1e-08) + 0.1 * weight
    )
    new_weight = weight - 0.001 * update
    return (summed, d_context, new_weight, new_moment_one, new_moment_two)


def solution(mesh):
    names = mesh.axis_names
    devices = mesh.devices.transpose([names.index("dp"), names.index("mp")])
    n_dp, n_mp = devices.shape
    split = Mesh(devices.reshape(n_dp // 2, 2, n_mp), ("chip", "core", "mp"))
    placed = (
        P(DP, "mp"),
        P(("mp",) + DP, None),
        P(("mp",) + DP, None),
        P(("mp",) + DP, None),
        P(DP + ("mp",), None),
    )
    return jax.shard_map(
        per_device,
        mesh=split,
        in_specs=placed,
        out_specs=(
            P(DP + ("mp",), None),
            P(DP, "mp"),
            P(("mp",) + DP, None),
            P(("mp",) + DP, None),
            P(("mp",) + DP, None),
        ),
        check_vma=False,
    )
```

```python
import math

import jax
import jax.numpy as jnp
import numpy as np
from jax import lax
from jax.sharding import Mesh
from jax.sharding import PartitionSpec as P

DP = ("chip", "core")


def chip_cycle(n):
    if n != 16:
        return list(range(n))
    order = []
    for i, (x, y) in enumerate(((0, 0), (1, 0), (1, 1), (0, 1))):
        for z in range(4) if i % 2 == 0 else range(3, -1, -1):
            order.append((z * 2 + y) * 2 + x)
    return order


def per_device(context, weight, moment_one, moment_two, grad_out):
    rows = weight.shape[0]
    tok_rows, local_cols = context.shape
    chips = lax.axis_size("chip")
    weight_bf = weight.astype(jnp.bfloat16)
    piece = lax.all_gather(grad_out, "mp", axis=0, tiled=True)
    width = piece.shape[1]
    swap = [(0, 1), (1, 0)]
    ctx_split = context.reshape(tok_rows, chips, 2, rows)
    me = lax.axis_index("core")
    ctx_own = jnp.where(me == 0, ctx_split[:, :, 0], ctx_split[:, :, 1]).reshape(tok_rows, chips * rows)
    ctx_other = jnp.where(me == 0, ctx_split[:, :, 1], ctx_split[:, :, 0]).reshape(tok_rows, chips * rows)
    dims_wgrad = (((0,), (0,)), ((), ()))

    full_weight = lax.all_gather(weight_bf, DP, axis=0, tiled=True)
    quarter = width // 4
    sums = []
    for q in range(4):
        piece_q = piece[:, q * quarter:(q + 1) * quarter]
        if sums:
            piece_q, _ = lax.optimization_barrier((piece_q, sums[-1]))
        grad_for_other = lax.dot_general(
            ctx_other, piece_q, dims_wgrad, preferred_element_type=jnp.float32
        ).astype(jnp.bfloat16)
        grad_from_other = lax.ppermute(grad_for_other, "core", swap)
        grad_mine = lax.dot_general(ctx_own, piece_q, dims_wgrad, preferred_element_type=jnp.float32)
        sums.append((grad_mine + grad_from_other.astype(jnp.float32)).astype(jnp.bfloat16))

    n = chips
    order = chip_cycle(n)
    position = [0] * n
    for i, c in enumerate(order):
        position[c] = i
    forward = [(order[i], order[(i + 1) % n]) for i in range(n)]
    backward = [(order[(i + 1) % n], order[i]) for i in range(n)]
    order_arr = jnp.asarray(np.array(order, np.int32))
    pos = jnp.asarray(np.array(position, np.int32))[lax.axis_index("chip")]
    half = width // 2

    def own_block(block, first):
        return jnp.concatenate(
            [lax.dynamic_slice_in_dim(sums[q], block * rows, rows, 0) for q in (first, first + 1)], axis=1
        ).astype(jnp.float32)

    n_pieces = 1
    out_cols = width // n_pieces
    d_rows = local_cols // n_pieces

    def product(j, w):
        if j < n_pieces:
            return jnp.dot(
                context, w[:, j * out_cols:(j + 1) * out_cols], preferred_element_type=jnp.float32
            ).astype(jnp.bfloat16)
        k = j - n_pieces
        return lax.dot_general(
            piece, w[k * d_rows:(k + 1) * d_rows], (((1,), (1,)), ((), ())),
            preferred_element_type=jnp.float32,
        ).astype(jnp.bfloat16)

    send_cw = own_block(order_arr[(pos - 1) % n], 0).astype(jnp.bfloat16)
    send_ccw = own_block(order_arr[(pos + 1) % n], 2).astype(jnp.bfloat16)
    products = []
    first_piece = max(0, n - 3 - 2 * n_pieces)
    for step in range(n - 1):
        recv_cw = lax.ppermute(send_cw, "chip", forward)
        recv_ccw = lax.ppermute(send_ccw, "chip", backward)
        j = step - first_piece
        if 0 <= j < 2 * n_pieces:
            w_now, _ = lax.optimization_barrier((full_weight, send_cw))
            products.append(product(j, w_now))
        mine_cw = own_block(order_arr[(pos - step - 2) % n], 0)
        mine_ccw = own_block(order_arr[(pos + step + 2) % n], 2)
        send_cw = (recv_cw.astype(jnp.float32) + mine_cw).astype(jnp.bfloat16)
        send_ccw = (recv_ccw.astype(jnp.float32) + mine_ccw).astype(jnp.bfloat16)
        if 0 <= j < 2 * n_pieces:
            send_cw, send_ccw, products[-1] = lax.optimization_barrier((send_cw, send_ccw, products[-1]))
    for j in range(len(products), 2 * n_pieces):
        products.append(product(j, full_weight))
    grad_shard = jnp.concatenate([send_cw, send_ccw], axis=1).astype(jnp.float32)
    out = jnp.concatenate(products[:n_pieces], axis=1)
    summed = lax.psum_scatter(out, "mp", scatter_dimension=0, tiled=True)
    d_context = jnp.concatenate(products[n_pieces:], axis=1)

    tokens_all = tok_rows * chips * 2
    grad = grad_shard * (1.0 / math.sqrt(tokens_all))
    new_moment_one = 0.9 * moment_one + 0.1 * grad
    new_moment_two = 0.999 * moment_two + 0.001 * grad * grad
    first_fix = 1.0 - 0.9**10
    second_fix = 1.0 - 0.999**10
    update = (
        new_moment_one / first_fix / (jnp.sqrt(new_moment_two / second_fix) + 1e-08) + 0.1 * weight
    )
    new_weight = weight - 0.001 * update
    return (summed, d_context, new_weight, new_moment_one, new_moment_two)


def solution(mesh):
    names = mesh.axis_names
    devices = mesh.devices.transpose([names.index("dp"), names.index("mp")])
    n_dp, n_mp = devices.shape
    split = Mesh(devices.reshape(n_dp // 2, 2, n_mp), ("chip", "core", "mp"))
    placed = (
        P(DP, "mp"),
        P(("mp",) + DP, None),
        P(("mp",) + DP, None),
        P(("mp",) + DP, None),
        P(DP + ("mp",), None),
    )
    return jax.shard_map(
        per_device,
        mesh=split,
        in_specs=placed,
        out_specs=(
            P(DP + ("mp",), None),
            P(DP, "mp"),
            P(("mp",) + DP, None),
            P(("mp",) + DP, None),
            P(("mp",) + DP, None),
        ),
        check_vma=False,
    )
```

```python
import math

import jax
import jax.numpy as jnp
import numpy as np
from jax import lax
from jax.sharding import Mesh
from jax.sharding import PartitionSpec as P

DP = ("chip", "core")


def chip_cycle(n):
    if n != 16:
        return list(range(n))
    order = []
    for i, (x, y) in enumerate(((0, 0), (1, 0), (1, 1), (0, 1))):
        for z in range(4) if i % 2 == 0 else range(3, -1, -1):
            order.append((z * 2 + y) * 2 + x)
    return order


def per_device(context, weight, moment_one, moment_two, grad_out):
    rows = weight.shape[0]
    tok_rows, local_cols = context.shape
    chips = lax.axis_size("chip")
    weight_bf = weight.astype(jnp.bfloat16)
    piece = lax.all_gather(grad_out, "mp", axis=0, tiled=True)
    width = piece.shape[1]
    swap = [(0, 1), (1, 0)]
    ctx_split = context.reshape(tok_rows, chips, 2, rows)
    me = lax.axis_index("core")
    ctx_own = jnp.where(me == 0, ctx_split[:, :, 0], ctx_split[:, :, 1]).reshape(tok_rows, chips * rows)
    ctx_other = jnp.where(me == 0, ctx_split[:, :, 1], ctx_split[:, :, 0]).reshape(tok_rows, chips * rows)
    dims_wgrad = (((0,), (0,)), ((), ()))

    full_weight = lax.all_gather(weight_bf, DP, axis=0, tiled=True)
    quarter = width // 4
    sums = []
    for q in range(4):
        piece_q = piece[:, q * quarter:(q + 1) * quarter]
        if sums:
            piece_q, _ = lax.optimization_barrier((piece_q, sums[-1]))
        grad_for_other = lax.dot_general(
            ctx_other, piece_q, dims_wgrad, preferred_element_type=jnp.float32
        ).astype(jnp.bfloat16)
        grad_from_other = lax.ppermute(grad_for_other, "core", swap)
        grad_mine = lax.dot_general(ctx_own, piece_q, dims_wgrad, preferred_element_type=jnp.float32)
        sums.append((grad_mine + grad_from_other.astype(jnp.float32)).astype(jnp.bfloat16))

    n = chips
    order = chip_cycle(n)
    position = [0] * n
    for i, c in enumerate(order):
        position[c] = i
    forward = [(order[i], order[(i + 1) % n]) for i in range(n)]
    backward = [(order[(i + 1) % n], order[i]) for i in range(n)]
    order_arr = jnp.asarray(np.array(order, np.int32))
    pos = jnp.asarray(np.array(position, np.int32))[lax.axis_index("chip")]
    half = width // 2

    def own_block(block, first):
        return jnp.concatenate(
            [lax.dynamic_slice_in_dim(sums[q], block * rows, rows, 0) for q in (first, first + 1)], axis=1
        ).astype(jnp.float32)

    n_pieces = 4
    out_cols = width // n_pieces
    d_rows = local_cols // n_pieces

    def product(j, w):
        if j < n_pieces:
            return jnp.dot(
                context, w[:, j * out_cols:(j + 1) * out_cols], preferred_element_type=jnp.float32
            ).astype(jnp.bfloat16)
        k = j - n_pieces
        return lax.dot_general(
            piece, w[k * d_rows:(k + 1) * d_rows], (((1,), (1,)), ((), ())),
            preferred_element_type=jnp.float32,
        ).astype(jnp.bfloat16)

    send_cw = own_block(order_arr[(pos - 1) % n], 0).astype(jnp.bfloat16)
    send_ccw = own_block(order_arr[(pos + 1) % n], 2).astype(jnp.bfloat16)
    products = []
    first_piece = max(0, n - 3 - 2 * n_pieces)
    for step in range(n - 1):
        recv_cw = lax.ppermute(send_cw, "chip", forward)
        recv_ccw = lax.ppermute(send_ccw, "chip", backward)
        j = step - first_piece
        if 0 <= j < 2 * n_pieces:
            w_now, _ = lax.optimization_barrier((full_weight, send_cw))
            products.append(product(j, w_now))
        mine_cw = own_block(order_arr[(pos - step - 2) % n], 0)
        mine_ccw = own_block(order_arr[(pos + step + 2) % n], 2)
        send_cw = (recv_cw.astype(jnp.float32) + mine_cw).astype(jnp.bfloat16)
        send_ccw = (recv_ccw.astype(jnp.float32) + mine_ccw).astype(jnp.bfloat16)
        if 0 <= j < 2 * n_pieces:
            send_cw, send_ccw, products[-1] = lax.optimization_barrier((send_cw, send_ccw, products[-1]))
    for j in range(len(products), 2 * n_pieces):
        products.append(product(j, full_weight))
    grad_shard = jnp.concatenate([send_cw, send_ccw], axis=1).astype(jnp.float32)
    out = jnp.concatenate(products[:n_pieces], axis=1)
    summed = lax.psum_scatter(out, "mp", scatter_dimension=0, tiled=True)
    d_context = jnp.concatenate(products[n_pieces:], axis=1)

    tokens_all = tok_rows * chips * 2
    grad = grad_shard * (1.0 / math.sqrt(tokens_all))
    new_moment_one = 0.9 * moment_one + 0.1 * grad
    new_moment_two = 0.999 * moment_two + 0.001 * grad * grad
    first_fix = 1.0 - 0.9**10
    second_fix = 1.0 - 0.999**10
    update = (
        new_moment_one / first_fix / (jnp.sqrt(new_moment_two / second_fix) + 1e-08) + 0.1 * weight
    )
    new_weight = weight - 0.001 * update
    return (summed, d_context, new_weight, new_moment_one, new_moment_two)


def solution(mesh):
    names = mesh.axis_names
    devices = mesh.devices.transpose([names.index("dp"), names.index("mp")])
    n_dp, n_mp = devices.shape
    split = Mesh(devices.reshape(n_dp // 2, 2, n_mp), ("chip", "core", "mp"))
    placed = (
        P(DP, "mp"),
        P(("mp",) + DP, None),
        P(("mp",) + DP, None),
        P(("mp",) + DP, None),
        P(DP + ("mp",), None),
    )
    return jax.shard_map(
        per_device,
        mesh=split,
        in_specs=placed,
        out_specs=(
            P(DP + ("mp",), None),
            P(DP, "mp"),
            P(("mp",) + DP, None),
            P(("mp",) + DP, None),
            P(("mp",) + DP, None),
        ),
        check_vma=False,
    )
```
